512 devices in a mesh: group: 16 (over x_lo, z), row: 32 (over x_hi, y, core).
Axes of the slice: x: 4 (x_hi: 2, x_lo: 2; x = x_hi * 2 + x_lo), y: 8, z: 8, core: 2. Of those that a mesh axis runs over, the one named last changes fastest.
Arguments:
- features: float32 [98304, 2048], P('row', 'group'), may hold values from -6 to 6
- feature_id: int32 [2048], P('group'), may hold values from 0 to 2047, each once
- feature_shift: float32 [2048], replicated, may hold values from -3 to 3
- feature_scale: float32 [2048], replicated, may hold values from 0.25 to 2
- proj_weight: bfloat16 [2048, 256], P('group'), may hold values from -0.5 to 0.5
- row_slot: int32 [32, 3072], P('row'), may hold values from 0 to 3071, each once within a row
- down_weight: bfloat16 [2, 4096, 128], P(None, 'row'), may hold values from -0.09375 to 0.09375
- up_weight: bfloat16 [2, 4096, 128], P(None, 'row'), may hold values from -0.5 to 0.5
- cross_bias: float32 [2, 4096], replicated, may hold values from -3 to 3
- head_weight: float32 [4096], replicated, may hold values from -0.09375 to 0.09375
- labels: int32 [98304], P(('group', 'row')), may hold values 0 or 1
Outputs:
- logits: float32 [98304], P(('group', 'row'))
- grad_down: float32 [2, 4096, 128], P(None, 'row')
- grad_up: float32 [2, 4096, 128], P(None, 'row')
- grad_bias: float32 [2, 4096], replicated
- grad_proj: float32 [2048, 256], P('group')
The draws below stay inside these ranges and needn't reach their ends.
Inputs may be any that keep to these rules, and one draw needn't show every extreme that they name: Each row of row_slot holds every number 0 .. 3071 once. feature_id holds every number 0 .. 2047 once.
All inputs are finite; a program needn't handle non-finite values. No bound on the sum of `labels` on one device may be relied on, other than what follows from the above.
Results may differ from the reference program's by a relative error of at most 0.02.
Values may be sent and summed in bfloat16 or wider, within the bound.
No kernel may reach another device: no remote copies, remote signals or barrier semaphores. Data moves between devices by JAX's collectives and lax.ppermute only.
A program may use at most 64 MiB of HBM per device.

```python
import math
import jax
import jax.numpy as jnp
from jax import lax

D = 4096
F = 2048
RANK = 128
LAYERS = 2
ROW_DEV = 192
FEAT_GROUP = 128
BLOCK = 256
SHARD_ROWS = 3072
SHARDS = 32
ROWS = 98304
N_GROUP = 16
N_ROW = 32


def place_ends(values, own_key, smallest, high):
    index_at = [jax.random.randint(jax.random.fold_in(own_key, axis), (), 0, length) for axis, length in enumerate(values.shape)]
    longest = values.shape.index(max(values.shape))
    next_to = index_at[:longest] + [(index_at[longest] + 1) % values.shape[longest]] + index_at[longest + 1:]
    return values.at[tuple(index_at)].set(smallest).at[tuple(next_to)].set(high)


def with_spikes(result, rng, source, target, parts, factor):
    def block_of(dim):
        return (jnp.arange(result.shape[dim]) // (result.shape[dim] // parts)).reshape((-1,) + (1,) * (result.ndim - 1 - dim))

    near = jax.random.permutation(rng, parts)[block_of(target)]
    other_side = (block_of(target) + parts // 2) % parts
    return jnp.where((block_of(source) == near) | (block_of(source) == other_side), factor * result, result)


def block_scale(rng, dims, cuts, least, largest):
    def one(position, parts):
        draws = jax.random.uniform(jax.random.fold_in(jax.random.fold_in(rng, 6), position), (parts,), jnp.float32, least / len(cuts), largest / len(cuts))
        return jnp.repeat(jnp.exp(draws), dims[position] // parts).reshape((-1,) + (1,) * (len(dims) - position - 1))

    factor_of = one(*cuts[0])
    for cut in cuts[1:]:
        factor_of = factor_of * one(*cut)
    return factor_of


def noise(own_key, shape, deviation, bound, split=(), held_as=jnp.bfloat16):
    result = jax.random.normal(own_key, shape, jnp.float32) * deviation
    if len(split) > 0:
        result = block_scale(own_key, shape, split, -0.22, 0.18) * result
    return jnp.clip(result, min=-bound, max=bound).astype(held_as)


def gaussian_with(own_key, dims, deviation, reach, cuts, heavy, held_as=jnp.bfloat16):
    entries = deviation * jax.random.normal(own_key, dims, jnp.float32)
    if cuts:
        entries = entries * block_scale(own_key, dims, cuts, -0.22, 0.18)
    return jnp.clip(with_spikes(entries, jax.random.fold_in(own_key, 3), *heavy), -reach, reach).astype(held_as)


def setup_inputs(seed: int = 0) -> dict:
    streams_of = jax.random.split(jax.random.key(seed), 12)
    return {
        "features": gaussian_with(streams_of[0], (ROWS, F), 1.0, 6.0, ((0, 32), (1, 16)), (0, 1, 32, 2.75), jnp.float32),
        "feature_id": jax.random.permutation(streams_of[1], F).astype(jnp.int32),
        "feature_shift": noise(streams_of[2], (F,), 0.7, 3.0, (), jnp.float32),
        "feature_scale": jnp.clip(jnp.exp(jax.random.uniform(streams_of[3], (F,), jnp.float32, math.log(0.25), math.log(2.0))), 0.25, 2.0),
        "proj_weight": noise(streams_of[4], (F, BLOCK), FEAT_GROUP ** -0.5, 0.5, ((0, 16),)),
        "row_slot": jax.vmap(lambda own: jax.random.permutation(own, SHARD_ROWS))(jax.random.split(streams_of[5], SHARDS)).reshape((SHARDS, SHARD_ROWS)).astype(jnp.int32),
        "down_weight": noise(streams_of[6], (LAYERS, D, RANK), D ** -0.5, 0.09375, ((1, 32),)),
        "up_weight": noise(streams_of[7], (LAYERS, D, RANK), RANK ** -0.5, 0.5, ((1, 32),)),
        "cross_bias": noise(streams_of[8], (LAYERS, D), 0.5, 3.0, (), jnp.float32),
        "head_weight": noise(streams_of[9], (D,), D ** -0.5, 0.09375, (), jnp.float32),
        "labels": place_ends((jax.random.randint(streams_of[10], (ROWS,), 0, 2) < 1).astype(jnp.int32), jax.random.fold_in(streams_of[10], 1), 0, 1),
    }


def rounded(term):
    return lax.optimization_barrier(term.astype(jnp.bfloat16)).astype(jnp.float32)


def reference(features, feature_id, feature_shift, feature_scale, proj_weight, row_slot,
              down_weight, up_weight, cross_bias, head_weight, labels):
    feat_group = F // N_GROUP
    block_width = D // N_GROUP
    shard_rows = ROW_DEV * N_GROUP
    highest = lax.Precision.HIGHEST
    column_shift = feature_shift[feature_id]
    column_scale = feature_scale[feature_id]
    positions = jnp.arange(shard_rows, dtype=jnp.int32)
    inverse = jnp.stack([jnp.zeros((shard_rows,), jnp.int32).at[row_slot[shard_index]].set(positions)
                         for shard_index in range(N_ROW)])
    split_weight = proj_weight.reshape(N_GROUP, feat_group, block_width).astype(jnp.float32)
    loss_scale = 2.0 * (D / ROWS) ** 0.5

    def one_block(carry, block_index):
        acc_down, acc_up, acc_bias, acc_proj = carry
        group_index = block_index // N_ROW
        shard_index = block_index % N_ROW
        shard_order = lax.dynamic_index_in_dim(inverse, shard_index, 0, keepdims=False)
        picked = lax.dynamic_slice_in_dim(shard_order, group_index * ROW_DEV, ROW_DEV)
        stored_rows = shard_index * shard_rows + picked
        raw_rows = features[stored_rows]
        normed = ((raw_rows - column_shift[None, :]) * column_scale[None, :]).astype(jnp.bfloat16)
        split_rows = normed.reshape(ROW_DEV, N_GROUP, feat_group).astype(jnp.float32)
        first = jnp.einsum("rgf,gfb->rgb", split_rows, split_weight, precision=highest)
        first = first.astype(jnp.bfloat16).reshape(ROW_DEV, D)
        first_wide = first.astype(jnp.float32)
        crossed = first
        stored = []
        for layer_index in range(LAYERS):
            hidden = jnp.dot(crossed, down_weight[layer_index], preferred_element_type=jnp.float32).astype(jnp.bfloat16)
            mixture = jnp.dot(hidden, up_weight[layer_index].T, preferred_element_type=jnp.float32) + cross_bias[layer_index][None, :]
            stored.append((crossed, hidden, mixture))
            crossed = (first_wide * mixture + crossed.astype(jnp.float32)).astype(jnp.bfloat16)
        logits = jnp.sum(crossed.astype(jnp.float32) * head_weight[None, :], axis=1)
        label_rows = lax.dynamic_slice_in_dim(labels, block_index * ROW_DEV, ROW_DEV)
        logit_grad = (jax.nn.sigmoid(logits) - label_rows.astype(jnp.float32)) * loss_scale
        back = (logit_grad[:, None] * head_weight[None, :]).astype(jnp.bfloat16)
        first_grad = jnp.zeros((ROW_DEV, D), jnp.float32)
        up_terms = [None] * LAYERS
        down_terms = [None] * LAYERS
        bias_terms = [None] * LAYERS
        for layer_index in reversed(range(LAYERS)):
            crossed_in, hidden, mixture = stored[layer_index]
            back_wide = back.astype(jnp.float32)
            first_grad = first_grad + back_wide * mixture
            mix_grad = (back_wide * first_wide).astype(jnp.bfloat16)
            up_terms[layer_index] = rounded(jnp.dot(mix_grad.T, hidden, preferred_element_type=jnp.float32))
            bias_terms[layer_index] = jnp.sum(mix_grad.astype(jnp.float32), axis=0)
            hidden_grad = jnp.dot(mix_grad, up_weight[layer_index], preferred_element_type=jnp.float32).astype(jnp.bfloat16)
            down_terms[layer_index] = rounded(jnp.dot(crossed_in.T, hidden_grad, preferred_element_type=jnp.float32))
            back = (back_wide + jnp.dot(hidden_grad, down_weight[layer_index].T, preferred_element_type=jnp.float32)).astype(jnp.bfloat16)
        first_grad = (first_grad + back.astype(jnp.float32)).astype(jnp.bfloat16)
        grad_split = first_grad.reshape(ROW_DEV, N_GROUP, block_width).astype(jnp.float32)
        proj_term = jnp.einsum("rgf,rgb->gfb", split_rows, grad_split, precision=highest)
        carry = (acc_down + jnp.stack(down_terms), acc_up + jnp.stack(up_terms),
                 acc_bias + jnp.stack(bias_terms), acc_proj + proj_term)
        return carry, logits

    start = (jnp.zeros((LAYERS, D, RANK), jnp.float32), jnp.zeros((LAYERS, D, RANK), jnp.float32),
             jnp.zeros((LAYERS, D), jnp.float32), jnp.zeros((N_GROUP, feat_group, block_width), jnp.float32))
    carry, logit_blocks = lax.scan(one_block, start, jnp.arange(N_GROUP * N_ROW, dtype=jnp.int32))
    acc_down, acc_up, acc_bias, acc_proj = carry
    return (logit_blocks.reshape(ROWS), acc_down, acc_up, acc_bias, acc_proj.reshape(F, block_width))
```

```python
import jax
import jax.numpy as jnp
from jax import lax
from jax.sharding import PartitionSpec as P


def column_table(feature_id, lookup_table):
    columns = jnp.arange(lookup_table.shape[0], dtype=jnp.int32)
    picker = (feature_id[:, None] == columns[None, :]).astype(jnp.float32)
    return jnp.dot(picker, lookup_table, precision=lax.Precision.HIGHEST)


def exchange_sum(partial, axis, count):
    pieces = partial.reshape(count, -1)
    mine = jnp.sum(lax.all_to_all(pieces, axis, 0, 0, tiled=True), axis=0)
    spread = jnp.broadcast_to(mine[None], pieces.shape)
    return lax.all_to_all(spread, axis, 0, 0, tiled=True).reshape(partial.shape)


def group_all_reduce(rows, groups):
    stacked, height, width = rows.shape
    pieces = rows.reshape(stacked, groups, height // groups, width).transpose(1, 0, 2, 3)
    mine = jnp.sum(lax.all_to_all(pieces, "group", 0, 0, tiled=True), axis=0)
    spread = jnp.broadcast_to(mine[None], pieces.shape)
    gathered = lax.all_to_all(spread, "group", 0, 0, tiled=True)
    return gathered.transpose(1, 0, 2, 3).reshape(rows.shape)


def body(
    features,
    feature_id,
    feature_shift,
    feature_scale,
    proj_weight,
    row_slot,
    down_weight,
    up_weight,
    cross_bias,
    head_weight,
    labels,
):
    layers = down_weight.shape[0]
    groups = lax.axis_size("group")
    row_count = labels.shape[0]
    feature_stats = column_table(feature_id, jnp.stack([feature_shift, feature_scale], axis=1))
    normed = ((features - feature_stats[:, 0][None, :]) * feature_stats[:, 1][None, :]).astype(
        jnp.bfloat16
    )
    ordered = jnp.zeros_like(normed).at[row_slot[0]].set(normed)
    projected = jnp.dot(ordered, proj_weight, preferred_element_type=jnp.float32).astype(
        jnp.bfloat16
    )
    first = lax.all_to_all(projected, "group", split_axis=0, concat_axis=1, tiled=True)
    first_wide = first.astype(jnp.float32)
    crossed = first
    stored = []
    weights_full = lax.all_gather(
        jnp.concatenate([down_weight, up_weight], axis=0), "row", axis=1, tiled=True
    )
    for layer_index in range(layers):
        down_full, up_full = weights_full[layer_index], weights_full[layers + layer_index]
        hidden = jnp.dot(crossed, down_full, preferred_element_type=jnp.float32).astype(
            jnp.bfloat16
        )
        mixture = lax.dot_general(
            hidden, up_full, (((1,), (1,)), ((), ())), preferred_element_type=jnp.float32
        )
        mixture = mixture + cross_bias[layer_index][None, :]
        stored.append((crossed, hidden, mixture, down_full, up_full))
        crossed = (first_wide * mixture + crossed.astype(jnp.float32)).astype(jnp.bfloat16)
    logits = jnp.sum(crossed.astype(jnp.float32) * head_weight[None, :], axis=1)
    total_rows = row_count * groups * lax.axis_size("row")
    loss_scale = 2.0 * (crossed.shape[1] / total_rows) ** 0.5
    logit_grad = (jax.nn.sigmoid(logits) - labels.astype(jnp.float32)) * loss_scale
    back = (logit_grad[:, None] * head_weight[None, :]).astype(jnp.bfloat16)
    first_grad = jnp.zeros(first.shape, jnp.float32)
    up_parts = [None] * layers
    down_parts = [None] * layers
    bias_terms = [None] * layers
    for layer_index in reversed(range(layers)):
        crossed_in, hidden, mixture, down_full, up_full = stored[layer_index]
        back_wide = back.astype(jnp.float32)
        first_grad = first_grad + back_wide * mixture
        mix_grad = (back_wide * first_wide).astype(jnp.bfloat16)
        up_term = lax.dot_general(
            mix_grad, hidden, (((0,), (0,)), ((), ())), preferred_element_type=jnp.float32
        )
        bias_terms[layer_index] = jnp.sum(mix_grad.astype(jnp.float32), axis=0)
        hidden_grad = jnp.dot(mix_grad, up_full, preferred_element_type=jnp.float32).astype(
            jnp.bfloat16
        )
        down_term = lax.dot_general(
            crossed_in, hidden_grad, (((0,), (0,)), ((), ())), preferred_element_type=jnp.float32
        )
        through = lax.dot_general(
            hidden_grad, down_full, (((1,), (1,)), ((), ())), preferred_element_type=jnp.float32
        )
        back = (back_wide + through).astype(jnp.bfloat16)
        up_parts[layer_index] = up_term
        down_parts[layer_index] = down_term
    weight_rows = lax.psum_scatter(
        jnp.stack(up_parts + down_parts).astype(jnp.bfloat16), "row", scatter_dimension=1, tiled=True
    )
    weight_sums = group_all_reduce(weight_rows.astype(jnp.float32), groups)
    grad_up, grad_down = weight_sums[:layers], weight_sums[layers:]
    first_grad = (first_grad + back.astype(jnp.float32)).astype(jnp.bfloat16)
    owner_grad = lax.all_to_all(first_grad, "group", split_axis=1, concat_axis=0, tiled=True)
    proj_term = lax.dot_general(
        ordered, owner_grad, (((0,), (0,)), ((), ())), preferred_element_type=jnp.float32
    )
    grad_proj = exchange_sum(proj_term, "row", lax.axis_size("row"))
    bias_all = jnp.stack(bias_terms)
    grad_bias = exchange_sum(bias_all, ("group", "row"), groups * lax.axis_size("row"))
    return (logits, grad_down, grad_up, grad_bias, grad_proj)


def solution(mesh):
    in_specs = (
        P("row", "group"),
        P("group"),
        P(),
        P(),
        P("group", None),
        P("row", None),
        P(None, "row", None),
        P(None, "row", None),
        P(),
        P(),
        P(("group", "row")),
    )
    out_specs = (
        P(("group", "row")),
        P(None, "row", None),
        P(None, "row", None),
        P(),
        P("group", None),
    )
    return jax.shard_map(body, mesh=mesh, in_specs=in_specs, out_specs=out_specs, check_vma=False)
```

```python
import jax
import jax.numpy as jnp
from jax import lax
from jax.sharding import PartitionSpec as P


def column_table(feature_id, lookup_table):
    columns = jnp.arange(lookup_table.shape[0], dtype=jnp.int32)
    picker = (feature_id[:, None] == columns[None, :]).astype(jnp.float32)
    return jnp.dot(picker, lookup_table, precision=lax.Precision.HIGHEST)


def body(
    features,
    feature_id,
    feature_shift,
    feature_scale,
    proj_weight,
    row_slot,
    down_weight,
    up_weight,
    cross_bias,
    head_weight,
    labels,
):
    layers = down_weight.shape[0]
    groups = lax.axis_size("group")
    row_count = labels.shape[0]
    feature_stats = column_table(feature_id, jnp.stack([feature_shift, feature_scale], axis=1))
    normed = ((features - feature_stats[:, 0][None, :]) * feature_stats[:, 1][None, :]).astype(
        jnp.bfloat16
    )
    ordered = jnp.zeros_like(normed).at[row_slot[0]].set(normed)
    projected = jnp.dot(ordered, proj_weight, preferred_element_type=jnp.float32).astype(
        jnp.bfloat16
    )
    first = lax.all_to_all(projected, "group", split_axis=0, concat_axis=1, tiled=True)
    first_wide = first.astype(jnp.float32)
    crossed = first
    stored = []
    weights_full = lax.all_gather(
        jnp.concatenate([down_weight, up_weight], axis=0), "row", axis=1, tiled=True
    )
    for layer_index in range(layers):
        down_full, up_full = weights_full[layer_index], weights_full[layers + layer_index]
        hidden = jnp.dot(crossed, down_full, preferred_element_type=jnp.float32).astype(
            jnp.bfloat16
        )
        mixture = lax.dot_general(
            hidden, up_full, (((1,), (1,)), ((), ())), preferred_element_type=jnp.float32
        )
        mixture = mixture + cross_bias[layer_index][None, :]
        stored.append((crossed, hidden, mixture, down_full, up_full))
        crossed = (first_wide * mixture + crossed.astype(jnp.float32)).astype(jnp.bfloat16)
    logits = jnp.sum(crossed.astype(jnp.float32) * head_weight[None, :], axis=1)
    total_rows = row_count * groups * lax.axis_size("row")
    loss_scale = 2.0 * (crossed.shape[1] / total_rows) ** 0.5
    logit_grad = (jax.nn.sigmoid(logits) - labels.astype(jnp.float32)) * loss_scale
    back = (logit_grad[:, None] * head_weight[None, :]).astype(jnp.bfloat16)
    first_grad = jnp.zeros(first.shape, jnp.float32)
    up_parts = [None] * layers
    down_parts = [None] * layers
    bias_terms = [None] * layers
    for layer_index in reversed(range(layers)):
        crossed_in, hidden, mixture, down_full, up_full = stored[layer_index]
        back_wide = back.astype(jnp.float32)
        first_grad = first_grad + back_wide * mixture
        mix_grad = (back_wide * first_wide).astype(jnp.bfloat16)
        up_term = lax.dot_general(
            mix_grad, hidden, (((0,), (0,)), ((), ())), preferred_element_type=jnp.float32
        )
        bias_terms[layer_index] = jnp.sum(mix_grad.astype(jnp.float32), axis=0)
        hidden_grad = jnp.dot(mix_grad, up_full, preferred_element_type=jnp.float32).astype(
            jnp.bfloat16
        )
        down_term = lax.dot_general(
            crossed_in, hidden_grad, (((0,), (0,)), ((), ())), preferred_element_type=jnp.float32
        )
        through = lax.dot_general(
            hidden_grad, down_full, (((1,), (1,)), ((), ())), preferred_element_type=jnp.float32
        )
        back = (back_wide + through).astype(jnp.bfloat16)
        up_parts[layer_index] = up_term
        down_parts[layer_index] = down_term
    row_count_axis = lax.axis_size("row")
    width = first.shape[1]
    rank = up_parts[0].shape[1]
    block_rows = width // row_count_axis
    piece = block_rows // groups
    bias_all = jnp.stack(bias_terms)
    bias_slab = jnp.zeros((row_count_axis, block_rows, rank), jnp.float32)
    bias_slab = bias_slab.at[:, :layers, :].set(
        bias_all.reshape(layers, row_count_axis, block_rows).transpose(1, 0, 2)
    )
    slabs = jnp.concatenate([jnp.stack(up_parts + down_parts), bias_slab.reshape(1, width, rank)])
    count = slabs.shape[0]
    slabs = slabs.astype(jnp.bfloat16).reshape(count, row_count_axis, groups, piece, rank)
    slabs = slabs.transpose(0, 2, 1, 3, 4).reshape(count, width, rank)
    group_part = lax.psum_scatter(slabs, "group", scatter_dimension=1, tiled=True)
    row_pieces = group_part.reshape(count, row_count_axis, piece, rank).transpose(1, 0, 2, 3)
    mine = jnp.sum(
        lax.all_to_all(row_pieces.astype(jnp.float32), "row", 0, 0, tiled=True), axis=0
    )
    spread = jnp.broadcast_to(mine[None], (groups,) + mine.shape)
    gathered = lax.all_to_all(spread, "group", 0, 0, tiled=True)
    blocks = gathered.transpose(1, 0, 2, 3).reshape(count, block_rows, rank)
    grad_up, grad_down = blocks[:layers], blocks[layers : 2 * layers]
    bias_rows = blocks[2 * layers, :layers, :]
    first_grad = (first_grad + back.astype(jnp.float32)).astype(jnp.bfloat16)
    owner_grad = lax.all_to_all(first_grad, "group", split_axis=1, concat_axis=0, tiled=True)
    proj_term = lax.dot_general(
        ordered, owner_grad, (((0,), (0,)), ((), ())), preferred_element_type=jnp.float32
    )
    proj_pieces = proj_term.reshape(row_count_axis, -1)
    proj_mine = jnp.sum(lax.all_to_all(proj_pieces, "row", 0, 0, tiled=True), axis=0)
    last = jnp.concatenate([proj_mine, bias_rows.reshape(-1)])
    last_all = lax.all_to_all(
        jnp.broadcast_to(last[None], (row_count_axis,) + last.shape), "row", 0, 0, tiled=True
    )
    grad_proj = last_all[:, : proj_mine.shape[0]].reshape(proj_term.shape)
    grad_bias = (
        last_all[:, proj_mine.shape[0] :]
        .reshape(row_count_axis, layers, block_rows)
        .transpose(1, 0, 2)
        .reshape(layers, width)
    )
    return (logits, grad_down, grad_up, grad_bias, grad_proj)


def solution(mesh):
    in_specs = (
        P("row", "group"),
        P("group"),
        P(),
        P(),
        P("group", None),
        P("row", None),
        P(None, "row", None),
        P(None, "row", None),
        P(),
        P(),
        P(("group", "row")),
    )
    out_specs = (
        P(("group", "row")),
        P(None, "row", None),
        P(None, "row", None),
        P(),
        P("group", None),
    )
    return jax.shard_map(body, mesh=mesh, in_specs=in_specs, out_specs=out_specs, check_vma=False)
```

```python
import jax
import jax.numpy as jnp
from jax import lax
from jax.sharding import PartitionSpec as P


def column_table(feature_id, lookup_table):
    columns = jnp.arange(lookup_table.shape[0], dtype=jnp.int32)
    picker = (feature_id[:, None] == columns[None, :]).astype(jnp.float32)
    return jnp.dot(picker, lookup_table, precision=lax.Precision.HIGHEST)


def exchange_sum(partial, axis, count):
    pieces = partial.reshape(count, -1)
    mine = jnp.sum(lax.all_to_all(pieces, axis, 0, 0, tiled=True), axis=0)
    spread = jnp.broadcast_to(mine[None], pieces.shape)
    return lax.all_to_all(spread, axis, 0, 0, tiled=True).reshape(partial.shape)


def body(
    features,
    feature_id,
    feature_shift,
    feature_scale,
    proj_weight,
    row_slot,
    down_weight,
    up_weight,
    cross_bias,
    head_weight,
    labels,
):
    layers = down_weight.shape[0]
    groups = lax.axis_size("group")
    row_count = labels.shape[0]
    feature_stats = column_table(feature_id, jnp.stack([feature_shift, feature_scale], axis=1))
    normed = ((features - feature_stats[:, 0][None, :]) * feature_stats[:, 1][None, :]).astype(
        jnp.bfloat16
    )
    ordered = jnp.zeros_like(normed).at[row_slot[0]].set(normed)
    projected = jnp.dot(ordered, proj_weight, preferred_element_type=jnp.float32).astype(
        jnp.bfloat16
    )
    first = lax.all_to_all(projected, "group", split_axis=0, concat_axis=1, tiled=True)
    first_wide = first.astype(jnp.float32)
    crossed = first
    stored = []
    weights_full = lax.all_gather(
        jnp.concatenate([down_weight, up_weight], axis=0), "row", axis=1, tiled=True
    )
    for layer_index in range(layers):
        down_full, up_full = weights_full[layer_index], weights_full[layers + layer_index]
        hidden = jnp.dot(crossed, down_full, preferred_element_type=jnp.float32).astype(
            jnp.bfloat16
        )
        mixture = lax.dot_general(
            hidden, up_full, (((1,), (1,)), ((), ())), preferred_element_type=jnp.float32
        )
        mixture = mixture + cross_bias[layer_index][None, :]
        stored.append((crossed, hidden, mixture, down_full, up_full))
        crossed = (first_wide * mixture + crossed.astype(jnp.float32)).astype(jnp.bfloat16)
    logits = jnp.sum(crossed.astype(jnp.float32) * head_weight[None, :], axis=1)
    total_rows = row_count * groups * lax.axis_size("row")
    loss_scale = 2.0 * (crossed.shape[1] / total_rows) ** 0.5
    logit_grad = (jax.nn.sigmoid(logits) - labels.astype(jnp.float32)) * loss_scale
    back = (logit_grad[:, None] * head_weight[None, :]).astype(jnp.bfloat16)
    first_grad = jnp.zeros(first.shape, jnp.float32)
    up_parts = [None] * layers
    down_parts = [None] * layers
    bias_terms = [None] * layers
    for layer_index in reversed(range(layers)):
        crossed_in, hidden, mixture, down_full, up_full = stored[layer_index]
        back_wide = back.astype(jnp.float32)
        first_grad = first_grad + back_wide * mixture
        mix_grad = (back_wide * first_wide).astype(jnp.bfloat16)
        up_term = lax.dot_general(
            mix_grad, hidden, (((0,), (0,)), ((), ())), preferred_element_type=jnp.float32
        )
        bias_terms[layer_index] = jnp.sum(mix_grad.astype(jnp.float32), axis=0)
        hidden_grad = jnp.dot(mix_grad, up_full, preferred_element_type=jnp.float32).astype(
            jnp.bfloat16
        )
        down_term = lax.dot_general(
            crossed_in, hidden_grad, (((0,), (0,)), ((), ())), preferred_element_type=jnp.float32
        )
        through = lax.dot_general(
            hidden_grad, down_full, (((1,), (1,)), ((), ())), preferred_element_type=jnp.float32
        )
        back = (back_wide + through).astype(jnp.bfloat16)
        up_parts[layer_index] = up_term
        down_parts[layer_index] = down_term
    row_count_axis = lax.axis_size("row")
    width = first.shape[1]
    rank = up_parts[0].shape[1]
    block_rows = width // row_count_axis
    piece = block_rows // groups
    slabs = jnp.stack(up_parts + down_parts).astype(jnp.bfloat16)
    count = slabs.shape[0]
    slabs = slabs.reshape(count, row_count_axis, groups, piece, rank).transpose(0, 2, 1, 3, 4)
    slabs = slabs.reshape(count, width, rank)
    group_part = lax.psum_scatter(slabs, "group", scatter_dimension=1, tiled=True)
    first_grad = (first_grad + back.astype(jnp.float32)).astype(jnp.bfloat16)
    owner_grad = lax.all_to_all(first_grad, "group", split_axis=1, concat_axis=0, tiled=True)
    proj_term = lax.dot_general(
        ordered, owner_grad, (((0,), (0,)), ((), ())), preferred_element_type=jnp.float32
    )
    grad_proj = exchange_sum(proj_term, "row", row_count_axis)
    grad_bias = exchange_sum(jnp.stack(bias_terms), ("group", "row"), groups * row_count_axis)
    group_part, grad_proj, grad_bias = lax.optimization_barrier((group_part, grad_proj, grad_bias))
    row_pieces = group_part.reshape(count, row_count_axis, piece, rank).transpose(1, 0, 2, 3)
    mine = jnp.sum(lax.all_to_all(row_pieces, "row", 0, 0, tiled=True).astype(jnp.float32), axis=0)
    spread = jnp.broadcast_to(mine[None], (groups,) + mine.shape)
    gathered = lax.all_to_all(spread, "group", 0, 0, tiled=True)
    blocks = gathered.transpose(1, 0, 2, 3).reshape(count, block_rows, rank)
    grad_up, grad_down = blocks[:layers], blocks[layers:]
    return (logits, grad_down, grad_up, grad_bias, grad_proj)


def solution(mesh):
    in_specs = (
        P("row", "group"),
        P("group"),
        P(),
        P(),
        P("group", None),
        P("row", None),
        P(None, "row", None),
        P(None, "row", None),
        P(),
        P(),
        P(("group", "row")),
    )
    out_specs = (
        P(("group", "row")),
        P(None, "row", None),
        P(None, "row", None),
        P(),
        P("group", None),
    )
    return jax.shard_map(body, mesh=mesh, in_specs=in_specs, out_specs=out_specs, check_vma=False)
```

```python
import jax
import jax.numpy as jnp
from jax import lax
from jax.sharding import PartitionSpec as P


def column_table(feature_id, lookup_table):
    columns = jnp.arange(lookup_table.shape[0], dtype=jnp.int32)
    picker = (feature_id[:, None] == columns[None, :]).astype(jnp.float32)
    return jnp.dot(picker, lookup_table, precision=lax.Precision.HIGHEST)


def body(
    features,
    feature_id,
    feature_shift,
    feature_scale,
    proj_weight,
    row_slot,
    down_weight,
    up_weight,
    cross_bias,
    head_weight,
    labels,
):
    layers = down_weight.shape[0]
    groups = lax.axis_size("group")
    row_count = labels.shape[0]
    feature_stats = column_table(feature_id, jnp.stack([feature_shift, feature_scale], axis=1))
    normed = ((features - feature_stats[:, 0][None, :]) * feature_stats[:, 1][None, :]).astype(
        jnp.bfloat16
    )
    ordered = jnp.zeros_like(normed).at[row_slot[0]].set(normed)
    projected = jnp.dot(ordered, proj_weight, preferred_element_type=jnp.float32).astype(
        jnp.bfloat16
    )
    first = lax.all_to_all(projected, "group", split_axis=0, concat_axis=1, tiled=True)
    first_wide = first.astype(jnp.float32)
    crossed = first
    stored = []
    weights_full = lax.all_gather(
        jnp.concatenate([down_weight, up_weight], axis=0), "row", axis=1, tiled=True
    )
    for layer_index in range(layers):
        down_full, up_full = weights_full[layer_index], weights_full[layers + layer_index]
        hidden = jnp.dot(crossed, down_full, preferred_element_type=jnp.float32).astype(
            jnp.bfloat16
        )
        mixture = lax.dot_general(
            hidden, up_full, (((1,), (1,)), ((), ())), preferred_element_type=jnp.float32
        )
        mixture = mixture + cross_bias[layer_index][None, :]
        stored.append((crossed, hidden, mixture, down_full, up_full))
        crossed = (first_wide * mixture + crossed.astype(jnp.float32)).astype(jnp.bfloat16)
    logits = jnp.sum(crossed.astype(jnp.float32) * head_weight[None, :], axis=1)
    total_rows = row_count * groups * lax.axis_size("row")
    loss_scale = 2.0 * (crossed.shape[1] / total_rows) ** 0.5
    logit_grad = (jax.nn.sigmoid(logits) - labels.astype(jnp.float32)) * loss_scale
    back = (logit_grad[:, None] * head_weight[None, :]).astype(jnp.bfloat16)
    first_grad = jnp.zeros(first.shape, jnp.float32)
    up_parts = [None] * layers
    down_parts = [None] * layers
    bias_terms = [None] * layers
    for layer_index in reversed(range(layers)):
        crossed_in, hidden, mixture, down_full, up_full = stored[layer_index]
        back_wide = back.astype(jnp.float32)
        first_grad = first_grad + back_wide * mixture
        mix_grad = (back_wide * first_wide).astype(jnp.bfloat16)
        up_term = lax.dot_general(
            mix_grad, hidden, (((0,), (0,)), ((), ())), preferred_element_type=jnp.float32
        )
        bias_terms[layer_index] = jnp.sum(mix_grad.astype(jnp.float32), axis=0)
        hidden_grad = jnp.dot(mix_grad, up_full, preferred_element_type=jnp.float32).astype(
            jnp.bfloat16
        )
        down_term = lax.dot_general(
            crossed_in, hidden_grad, (((0,), (0,)), ((), ())), preferred_element_type=jnp.float32
        )
        through = lax.dot_general(
            hidden_grad, down_full, (((1,), (1,)), ((), ())), preferred_element_type=jnp.float32
        )
        back = (back_wide + through).astype(jnp.bfloat16)
        up_parts[layer_index] = up_term
        down_parts[layer_index] = down_term
    row_count_axis = lax.axis_size("row")
    width = first.shape[1]
    rank = up_parts[0].shape[1]
    block_rows = width // row_count_axis
    piece = block_rows // groups
    bias_all = jnp.stack(bias_terms)
    bias_slab = jnp.pad(
        bias_all.reshape(layers, row_count_axis, block_rows).transpose(1, 0, 2),
        ((0, 0), (0, block_rows - layers), (0, rank - block_rows)),
    ).reshape(1, width, rank)
    slabs = jnp.concatenate([jnp.stack(up_parts + down_parts), bias_slab]).astype(jnp.bfloat16)
    count = slabs.shape[0]
    slabs = slabs.reshape(count, row_count_axis, groups, piece, rank).transpose(0, 2, 1, 3, 4)
    slabs = slabs.reshape(count, width, rank)
    group_part = lax.psum_scatter(slabs, "group", scatter_dimension=1, tiled=True)
    first_grad = (first_grad + back.astype(jnp.float32)).astype(jnp.bfloat16)
    owner_grad = lax.all_to_all(first_grad, "group", split_axis=1, concat_axis=0, tiled=True)
    proj_term = lax.dot_general(
        ordered, owner_grad, (((0,), (0,)), ((), ())), preferred_element_type=jnp.float32
    )
    proj_pieces = proj_term.reshape(row_count_axis, -1)
    proj_mine = jnp.sum(lax.all_to_all(proj_pieces, "row", 0, 0, tiled=True), axis=0)
    group_part, proj_mine = lax.optimization_barrier((group_part, proj_mine))
    row_pieces = group_part.reshape(count, row_count_axis, piece, rank).transpose(1, 0, 2, 3)
    mine = jnp.sum(lax.all_to_all(row_pieces, "row", 0, 0, tiled=True).astype(jnp.float32), axis=0)
    spread = jnp.broadcast_to(mine[None], (groups,) + mine.shape)
    gathered = lax.all_to_all(spread, "group", 0, 0, tiled=True)
    blocks = gathered.transpose(1, 0, 2, 3).reshape(count, block_rows, rank)
    grad_up, grad_down = blocks[:layers], blocks[layers : 2 * layers]
    bias_rows = blocks[2 * layers, :layers, :]
    last = jnp.concatenate([proj_mine, bias_rows.reshape(-1)])
    last_all = lax.all_to_all(
        jnp.broadcast_to(last[None], (row_count_axis,) + last.shape), "row", 0, 0, tiled=True
    )
    grad_proj = last_all[:, : proj_mine.shape[0]].reshape(proj_term.shape)
    grad_bias = (
        last_all[:, proj_mine.shape[0] :]
        .reshape(row_count_axis, layers, block_rows)
        .transpose(1, 0, 2)
        .reshape(layers, width)
    )
    return (logits, grad_down, grad_up, grad_bias, grad_proj)


def solution(mesh):
    in_specs = (
        P("row", "group"),
        P("group"),
        P(),
        P(),
        P("group", None),
        P("row", None),
        P(None, "row", None),
        P(None, "row", None),
        P(),
        P(),
        P(("group", "row")),
    )
    out_specs = (
        P(("group", "row")),
        P(None, "row", None),
        P(None, "row", None),
        P(),
        P("group", None),
    )
    return jax.shard_map(body, mesh=mesh, in_specs=in_specs, out_specs=out_specs, check_vma=False)
```

```python
import jax
import jax.numpy as jnp
from jax import lax
from jax.sharding import PartitionSpec as P


def column_table(feature_id, lookup_table):
    columns = jnp.arange(lookup_table.shape[0], dtype=jnp.int32)
    picker = (feature_id[:, None] == columns[None, :]).astype(jnp.float32)
    return jnp.dot(picker, lookup_table, precision=lax.Precision.HIGHEST)


def exchange_sum(partial, axis, count):
    pieces = partial.reshape(count, -1)
    mine = jnp.sum(lax.all_to_all(pieces, axis, 0, 0, tiled=True), axis=0)
    spread = jnp.broadcast_to(mine[None], pieces.shape)
    return lax.all_to_all(spread, axis, 0, 0, tiled=True).reshape(partial.shape)


def group_all_reduce(rows, groups):
    stacked, height, width = rows.shape
    pieces = rows.reshape(stacked, groups, height // groups, width).transpose(1, 0, 2, 3)
    mine = jnp.sum(lax.all_to_all(pieces, "group", 0, 0, tiled=True).astype(jnp.float32), axis=0)
    spread = jnp.broadcast_to(mine[None], pieces.shape)
    gathered = lax.all_to_all(spread, "group", 0, 0, tiled=True)
    return gathered.transpose(1, 0, 2, 3).reshape(rows.shape)


def body(
    features,
    feature_id,
    feature_shift,
    feature_scale,
    proj_weight,
    row_slot,
    down_weight,
    up_weight,
    cross_bias,
    head_weight,
    labels,
):
    layers = down_weight.shape[0]
    groups = lax.axis_size("group")
    row_count = labels.shape[0]
    feature_stats = column_table(feature_id, jnp.stack([feature_shift, feature_scale], axis=1))
    normed = ((features - feature_stats[:, 0][None, :]) * feature_stats[:, 1][None, :]).astype(
        jnp.bfloat16
    )
    ordered = jnp.zeros_like(normed).at[row_slot[0]].set(normed)
    projected = jnp.dot(ordered, proj_weight, preferred_element_type=jnp.float32).astype(
        jnp.bfloat16
    )
    first = lax.all_to_all(projected, "group", split_axis=0, concat_axis=1, tiled=True)
    first_wide = first.astype(jnp.float32)
    crossed = first
    stored = []
    weights_full = lax.all_gather(
        jnp.concatenate([down_weight, up_weight], axis=0), "row", axis=1, tiled=True
    )
    for layer_index in range(layers):
        down_full, up_full = weights_full[layer_index], weights_full[layers + layer_index]
        hidden = jnp.dot(crossed, down_full, preferred_element_type=jnp.float32).astype(
            jnp.bfloat16
        )
        mixture = lax.dot_general(
            hidden, up_full, (((1,), (1,)), ((), ())), preferred_element_type=jnp.float32
        )
        mixture = mixture + cross_bias[layer_index][None, :]
        stored.append((crossed, hidden, mixture, down_full, up_full))
        crossed = (first_wide * mixture + crossed.astype(jnp.float32)).astype(jnp.bfloat16)
    logits = jnp.sum(crossed.astype(jnp.float32) * head_weight[None, :], axis=1)
    total_rows = row_count * groups * lax.axis_size("row")
    loss_scale = 2.0 * (crossed.shape[1] / total_rows) ** 0.5
    logit_grad = (jax.nn.sigmoid(logits) - labels.astype(jnp.float32)) * loss_scale
    back = (logit_grad[:, None] * head_weight[None, :]).astype(jnp.bfloat16)
    first_grad = jnp.zeros(first.shape, jnp.float32)
    up_parts = [None] * layers
    down_parts = [None] * layers
    bias_terms = [None] * layers
    for layer_index in reversed(range(layers)):
        crossed_in, hidden, mixture, down_full, up_full = stored[layer_index]
        back_wide = back.astype(jnp.float32)
        first_grad = first_grad + back_wide * mixture
        mix_grad = (back_wide * first_wide).astype(jnp.bfloat16)
        up_term = lax.dot_general(
            mix_grad, hidden, (((0,), (0,)), ((), ())), preferred_element_type=jnp.float32
        )
        bias_terms[layer_index] = jnp.sum(mix_grad.astype(jnp.float32), axis=0)
        hidden_grad = jnp.dot(mix_grad, up_full, preferred_element_type=jnp.float32).astype(
            jnp.bfloat16
        )
        down_term = lax.dot_general(
            crossed_in, hidden_grad, (((0,), (0,)), ((), ())), preferred_element_type=jnp.float32
        )
        through = lax.dot_general(
            hidden_grad, down_full, (((1,), (1,)), ((), ())), preferred_element_type=jnp.float32
        )
        back = (back_wide + through).astype(jnp.bfloat16)
        up_parts[layer_index] = up_term
        down_parts[layer_index] = down_term
    weight_rows = lax.psum_scatter(
        jnp.stack(up_parts + down_parts).astype(jnp.bfloat16), "row", scatter_dimension=1, tiled=True
    )
    first_grad = (first_grad + back.astype(jnp.float32)).astype(jnp.bfloat16)
    owner_grad = lax.all_to_all(first_grad, "group", split_axis=1, concat_axis=0, tiled=True)
    proj_term = lax.dot_general(
        ordered, owner_grad, (((0,), (0,)), ((), ())), preferred_element_type=jnp.float32
    )
    grad_proj = exchange_sum(proj_term, "row", lax.axis_size("row"))
    bias_all = jnp.stack(bias_terms)
    grad_bias = exchange_sum(bias_all, ("group", "row"), groups * lax.axis_size("row"))
    weight_rows, grad_proj, grad_bias = lax.optimization_barrier((weight_rows, grad_proj, grad_bias))
    weight_sums = group_all_reduce(weight_rows, groups)
    grad_up, grad_down = weight_sums[:layers], weight_sums[layers:]
    return (logits, grad_down, grad_up, grad_bias, grad_proj)


def solution(mesh):
    in_specs = (
        P("row", "group"),
        P("group"),
        P(),
        P(),
        P("group", None),
        P("row", None),
        P(None, "row", None),
        P(None, "row", None),
        P(),
        P(),
        P(("group", "row")),
    )
    out_specs = (
        P(("group", "row")),
        P(None, "row", None),
        P(None, "row", None),
        P(),
        P("group", None),
    )
    return jax.shard_map(body, mesh=mesh, in_specs=in_specs, out_specs=out_specs, check_vma=False)
```

```python
import jax
import jax.numpy as jnp
from jax import lax
from jax.sharding import PartitionSpec as P


def column_table(feature_id, lookup_table):
    columns = jnp.arange(lookup_table.shape[0], dtype=jnp.int32)
    picker = (feature_id[:, None] == columns[None, :]).astype(jnp.float32)
    return jnp.dot(picker, lookup_table, precision=lax.Precision.HIGHEST)


def exchange_sum(partial, axis, count):
    pieces = partial.reshape(count, -1)
    mine = jnp.sum(lax.all_to_all(pieces, axis, 0, 0, tiled=True), axis=0)
    spread = jnp.broadcast_to(mine[None], pieces.shape)
    return lax.all_to_all(spread, axis, 0, 0, tiled=True).reshape(partial.shape)


def group_all_reduce(rows, groups):
    stacked, height, width = rows.shape
    pieces = rows.reshape(stacked, groups, height // groups, width).transpose(1, 0, 2, 3)
    mine = jnp.sum(lax.all_to_all(pieces, "group", 0, 0, tiled=True).astype(jnp.float32), axis=0)
    spread = jnp.broadcast_to(mine[None], pieces.shape)
    gathered = lax.all_to_all(spread, "group", 0, 0, tiled=True)
    return gathered.transpose(1, 0, 2, 3).reshape(rows.shape)


def doubling_gather(shard, axis):
    count = lax.axis_size(axis)
    me = lax.axis_index(axis)
    held = shard[:, None]
    step = 1
    while step < count:
        pairs = [(i, i ^ step) for i in range(count)]
        other = lax.ppermute(held, axis, pairs)
        upper = (me // step) % 2
        held = jnp.where(upper == 1, jnp.concatenate([other, held], axis=1), jnp.concatenate([held, other], axis=1))
        step *= 2
    return held.reshape(shard.shape[0], count * shard.shape[1], *shard.shape[2:])


def body(
    features,
    feature_id,
    feature_shift,
    feature_scale,
    proj_weight,
    row_slot,
    down_weight,
    up_weight,
    cross_bias,
    head_weight,
    labels,
):
    layers = down_weight.shape[0]
    groups = lax.axis_size("group")
    row_count = labels.shape[0]
    feature_stats = column_table(feature_id, jnp.stack([feature_shift, feature_scale], axis=1))
    normed = ((features - feature_stats[:, 0][None, :]) * feature_stats[:, 1][None, :]).astype(
        jnp.bfloat16
    )
    ordered = jnp.zeros_like(normed).at[row_slot[0]].set(normed)
    projected = jnp.dot(ordered, proj_weight, preferred_element_type=jnp.float32).astype(
        jnp.bfloat16
    )
    first = lax.all_to_all(projected, "group", split_axis=0, concat_axis=1, tiled=True)
    first_wide = first.astype(jnp.float32)
    crossed = first
    stored = []
    weights_full = doubling_gather(jnp.concatenate([down_weight, up_weight], axis=0), "row")
    for layer_index in range(layers):
        down_full, up_full = weights_full[layer_index], weights_full[layers + layer_index]
        hidden = jnp.dot(crossed, down_full, preferred_element_type=jnp.float32).astype(
            jnp.bfloat16
        )
        mixture = lax.dot_general(
            hidden, up_full, (((1,), (1,)), ((), ())), preferred_element_type=jnp.float32
        )
        mixture = mixture + cross_bias[layer_index][None, :]
        stored.append((crossed, hidden, mixture, down_full, up_full))
        crossed = (first_wide * mixture + crossed.astype(jnp.float32)).astype(jnp.bfloat16)
    logits = jnp.sum(crossed.astype(jnp.float32) * head_weight[None, :], axis=1)
    total_rows = row_count * groups * lax.axis_size("row")
    loss_scale = 2.0 * (crossed.shape[1] / total_rows) ** 0.5
    logit_grad = (jax.nn.sigmoid(logits) - labels.astype(jnp.float32)) * loss_scale
    back = (logit_grad[:, None] * head_weight[None, :]).astype(jnp.bfloat16)
    first_grad = jnp.zeros(first.shape, jnp.float32)
    up_parts = [None] * layers
    down_parts = [None] * layers
    bias_terms = [None] * layers
    for layer_index in reversed(range(layers)):
        crossed_in, hidden, mixture, down_full, up_full = stored[layer_index]
        back_wide = back.astype(jnp.float32)
        first_grad = first_grad + back_wide * mixture
        mix_grad = (back_wide * first_wide).astype(jnp.bfloat16)
        up_term = lax.dot_general(
            mix_grad, hidden, (((0,), (0,)), ((), ())), preferred_element_type=jnp.float32
        )
        bias_terms[layer_index] = jnp.sum(mix_grad.astype(jnp.float32), axis=0)
        hidden_grad = jnp.dot(mix_grad, up_full, preferred_element_type=jnp.float32).astype(
            jnp.bfloat16
        )
        down_term = lax.dot_general(
            crossed_in, hidden_grad, (((0,), (0,)), ((), ())), preferred_element_type=jnp.float32
        )
        through = lax.dot_general(
            hidden_grad, down_full, (((1,), (1,)), ((), ())), preferred_element_type=jnp.float32
        )
        back = (back_wide + through).astype(jnp.bfloat16)
        up_parts[layer_index] = up_term
        down_parts[layer_index] = down_term
    weight_rows = lax.psum_scatter(
        jnp.stack(up_parts + down_parts).astype(jnp.bfloat16), "row", scatter_dimension=1, tiled=True
    )
    first_grad = (first_grad + back.astype(jnp.float32)).astype(jnp.bfloat16)
    owner_grad = lax.all_to_all(first_grad, "group", split_axis=1, concat_axis=0, tiled=True)
    proj_term = lax.dot_general(
        ordered, owner_grad, (((0,), (0,)), ((), ())), preferred_element_type=jnp.float32
    )
    grad_proj = exchange_sum(proj_term, "row", lax.axis_size("row"))
    bias_all = jnp.stack(bias_terms)
    grad_bias = exchange_sum(bias_all, ("group", "row"), groups * lax.axis_size("row"))
    weight_rows, grad_proj, grad_bias = lax.optimization_barrier((weight_rows, grad_proj, grad_bias))
    weight_sums = group_all_reduce(weight_rows, groups)
    grad_up, grad_down = weight_sums[:layers], weight_sums[layers:]
    return (logits, grad_down, grad_up, grad_bias, grad_proj)


def solution(mesh):
    in_specs = (
        P("row", "group"),
        P("group"),
        P(),
        P(),
        P("group", None),
        P("row", None),
        P(None, "row", None),
        P(None, "row", None),
        P(),
        P(),
        P(("group", "row")),
    )
    out_specs = (
        P(("group", "row")),
        P(None, "row", None),
        P(None, "row", None),
        P(),
        P("group", None),
    )
    return jax.shard_map(body, mesh=mesh, in_specs=in_specs, out_specs=out_specs, check_vma=False)
```

```python
import jax
import jax.numpy as jnp
from jax import lax
from jax.sharding import PartitionSpec as P


def column_table(feature_id, lookup_table):
    columns = jnp.arange(lookup_table.shape[0], dtype=jnp.int32)
    picker = (feature_id[:, None] == columns[None, :]).astype(jnp.float32)
    return jnp.dot(picker, lookup_table, precision=lax.Precision.HIGHEST)


def exchange_sum(partial, axis, count):
    pieces = partial.reshape(count, -1)
    mine = jnp.sum(lax.all_to_all(pieces, axis, 0, 0, tiled=True), axis=0)
    spread = jnp.broadcast_to(mine[None], pieces.shape)
    return lax.all_to_all(spread, axis, 0, 0, tiled=True).reshape(partial.shape)


def group_all_reduce(rows, groups):
    stacked, height, width = rows.shape
    pieces = rows.reshape(stacked, groups, height // groups, width).transpose(1, 0, 2, 3)
    mine = jnp.sum(lax.all_to_all(pieces, "group", 0, 0, tiled=True).astype(jnp.float32), axis=0)
    spread = jnp.broadcast_to(mine[None], pieces.shape)
    gathered = lax.all_to_all(spread, "group", 0, 0, tiled=True)
    return gathered.transpose(1, 0, 2, 3).reshape(rows.shape)


def body(
    features,
    feature_id,
    feature_shift,
    feature_scale,
    proj_weight,
    row_slot,
    down_weight,
    up_weight,
    cross_bias,
    head_weight,
    labels,
):
    layers = down_weight.shape[0]
    groups = lax.axis_size("group")
    row_count = labels.shape[0]
    feature_stats = column_table(feature_id, jnp.stack([feature_shift, feature_scale], axis=1))
    normed = ((features - feature_stats[:, 0][None, :]) * feature_stats[:, 1][None, :]).astype(
        jnp.bfloat16
    )
    ordered = jnp.zeros_like(normed).at[row_slot[0]].set(normed)
    projected = jnp.dot(ordered, proj_weight, preferred_element_type=jnp.float32).astype(
        jnp.bfloat16
    )
    first = lax.all_to_all(projected, "group", split_axis=0, concat_axis=1, tiled=True)
    first_wide = first.astype(jnp.float32)
    crossed = first
    stored = []
    weights_full = lax.all_gather(
        jnp.concatenate([down_weight, up_weight], axis=0), "row", axis=1, tiled=True
    )
    for layer_index in range(layers):
        down_full, up_full = weights_full[layer_index], weights_full[layers + layer_index]
        hidden = jnp.dot(crossed, down_full, preferred_element_type=jnp.float32).astype(
            jnp.bfloat16
        )
        mixture = lax.dot_general(
            hidden, up_full, (((1,), (1,)), ((), ())), preferred_element_type=jnp.float32
        )
        mixture = mixture + cross_bias[layer_index][None, :]
        stored.append((crossed, hidden, mixture, down_full, up_full))
        crossed = (first_wide * mixture + crossed.astype(jnp.float32)).astype(jnp.bfloat16)
    logits = jnp.sum(crossed.astype(jnp.float32) * head_weight[None, :], axis=1)
    total_rows = row_count * groups * lax.axis_size("row")
    loss_scale = 2.0 * (crossed.shape[1] / total_rows) ** 0.5
    logit_grad = (jax.nn.sigmoid(logits) - labels.astype(jnp.float32)) * loss_scale
    back = (logit_grad[:, None] * head_weight[None, :]).astype(jnp.bfloat16)
    first_grad = jnp.zeros(first.shape, jnp.float32)
    up_parts = [None] * layers
    down_parts = [None] * layers
    bias_terms = [None] * layers
    for layer_index in reversed(range(layers)):
        crossed_in, hidden, mixture, down_full, up_full = stored[layer_index]
        back_wide = back.astype(jnp.float32)
        first_grad = first_grad + back_wide * mixture
        mix_grad = (back_wide * first_wide).astype(jnp.bfloat16)
        up_term = lax.dot_general(
            mix_grad, hidden, (((0,), (0,)), ((), ())), preferred_element_type=jnp.float32
        )
        bias_terms[layer_index] = jnp.sum(mix_grad.astype(jnp.float32), axis=0)
        hidden_grad = jnp.dot(mix_grad, up_full, preferred_element_type=jnp.float32).astype(
            jnp.bfloat16
        )
        down_term = lax.dot_general(
            crossed_in, hidden_grad, (((0,), (0,)), ((), ())), preferred_element_type=jnp.float32
        )
        through = lax.dot_general(
            hidden_grad, down_full, (((1,), (1,)), ((), ())), preferred_element_type=jnp.float32
        )
        back = (back_wide + through).astype(jnp.bfloat16)
        up_parts[layer_index] = up_term
        down_parts[layer_index] = down_term
    weight_rows = lax.psum_scatter(
        jnp.stack(up_parts + down_parts).astype(jnp.bfloat16), "row", scatter_dimension=1, tiled=True
    )
    first_grad = (first_grad + back.astype(jnp.float32)).astype(jnp.bfloat16)
    owner_grad = lax.all_to_all(first_grad, "group", split_axis=1, concat_axis=0, tiled=True)
    proj_term = lax.dot_general(
        ordered, owner_grad, (((0,), (0,)), ((), ())), preferred_element_type=jnp.float32
    )
    row_count_axis = lax.axis_size("row")
    bias_all = jnp.stack(bias_terms)
    proj_pieces = proj_term.reshape(row_count_axis, -1)
    bias_pieces = bias_all.reshape(layers, row_count_axis, -1).transpose(1, 0, 2)
    bias_pieces = bias_pieces.reshape(row_count_axis, -1)
    split = proj_pieces.shape[1]
    row_mine = jnp.sum(
        lax.all_to_all(jnp.concatenate([proj_pieces, bias_pieces], axis=1), "row", 0, 0, tiled=True),
        axis=0,
    )
    bias_chunk = exchange_sum(row_mine[split:], "group", groups)
    last = jnp.concatenate([row_mine[:split], bias_chunk])
    last_all = lax.all_to_all(
        jnp.broadcast_to(last[None], (row_count_axis,) + last.shape), "row", 0, 0, tiled=True
    )
    grad_proj = last_all[:, :split].reshape(proj_term.shape)
    grad_bias = (
        last_all[:, split:]
        .reshape(row_count_axis, layers, -1)
        .transpose(1, 0, 2)
        .reshape(bias_all.shape)
    )
    weight_rows, grad_proj, grad_bias = lax.optimization_barrier((weight_rows, grad_proj, grad_bias))
    weight_sums = group_all_reduce(weight_rows, groups)
    grad_up, grad_down = weight_sums[:layers], weight_sums[layers:]
    return (logits, grad_down, grad_up, grad_bias, grad_proj)


def solution(mesh):
    in_specs = (
        P("row", "group"),
        P("group"),
        P(),
        P(),
        P("group", None),
        P("row", None),
        P(None, "row", None),
        P(None, "row", None),
        P(),
        P(),
        P(("group", "row")),
    )
    out_specs = (
        P(("group", "row")),
        P(None, "row", None),
        P(None, "row", None),
        P(),
        P("group", None),
    )
    return jax.shard_map(body, mesh=mesh, in_specs=in_specs, out_specs=out_specs, check_vma=False)
```

```python
import jax
import jax.numpy as jnp
from jax import lax
from jax.sharding import PartitionSpec as P


def column_table(feature_id, lookup_table):
    columns = jnp.arange(lookup_table.shape[0], dtype=jnp.int32)
    picker = (feature_id[:, None] == columns[None, :]).astype(jnp.float32)
    return jnp.dot(picker, lookup_table, precision=lax.Precision.HIGHEST)


def exchange_sum(partial, axis, count):
    pieces = partial.reshape(count, -1)
    mine = jnp.sum(lax.all_to_all(pieces, axis, 0, 0, tiled=True), axis=0)
    spread = jnp.broadcast_to(mine[None], pieces.shape)
    return lax.all_to_all(spread, axis, 0, 0, tiled=True).reshape(partial.shape)


def body(
    features,
    feature_id,
    feature_shift,
    feature_scale,
    proj_weight,
    row_slot,
    down_weight,
    up_weight,
    cross_bias,
    head_weight,
    labels,
):
    layers = down_weight.shape[0]
    groups = lax.axis_size("group")
    row_count = labels.shape[0]
    feature_stats = column_table(feature_id, jnp.stack([feature_shift, feature_scale], axis=1))
    normed = ((features - feature_stats[:, 0][None, :]) * feature_stats[:, 1][None, :]).astype(
        jnp.bfloat16
    )
    ordered = jnp.zeros_like(normed).at[row_slot[0]].set(normed)
    projected = jnp.dot(ordered, proj_weight, preferred_element_type=jnp.float32).astype(
        jnp.bfloat16
    )
    first = lax.all_to_all(projected, "group", split_axis=0, concat_axis=1, tiled=True)
    first_wide = first.astype(jnp.float32)
    crossed = first
    stored = []
    weights_full = lax.all_gather(
        jnp.concatenate([down_weight, up_weight], axis=0), "row", axis=1, tiled=True
    )
    for layer_index in range(layers):
        down_full, up_full = weights_full[layer_index], weights_full[layers + layer_index]
        hidden = jnp.dot(crossed, down_full, preferred_element_type=jnp.float32).astype(
            jnp.bfloat16
        )
        mixture = lax.dot_general(
            hidden, up_full, (((1,), (1,)), ((), ())), preferred_element_type=jnp.float32
        )
        mixture = mixture + cross_bias[layer_index][None, :]
        stored.append((crossed, hidden, mixture, down_full, up_full))
        crossed = (first_wide * mixture + crossed.astype(jnp.float32)).astype(jnp.bfloat16)
    logits = jnp.sum(crossed.astype(jnp.float32) * head_weight[None, :], axis=1)
    total_rows = row_count * groups * lax.axis_size("row")
    loss_scale = 2.0 * (crossed.shape[1] / total_rows) ** 0.5
    logit_grad = (jax.nn.sigmoid(logits) - labels.astype(jnp.float32)) * loss_scale
    back = (logit_grad[:, None] * head_weight[None, :]).astype(jnp.bfloat16)
    first_grad = jnp.zeros(first.shape, jnp.float32)
    up_parts = [None] * layers
    down_parts = [None] * layers
    bias_terms = [None] * layers
    for layer_index in reversed(range(layers)):
        crossed_in, hidden, mixture, down_full, up_full = stored[layer_index]
        back_wide = back.astype(jnp.float32)
        first_grad = first_grad + back_wide * mixture
        mix_grad = (back_wide * first_wide).astype(jnp.bfloat16)
        up_term = lax.dot_general(
            mix_grad, hidden, (((0,), (0,)), ((), ())), preferred_element_type=jnp.float32
        )
        bias_terms[layer_index] = jnp.sum(mix_grad.astype(jnp.float32), axis=0)
        hidden_grad = jnp.dot(mix_grad, up_full, preferred_element_type=jnp.float32).astype(
            jnp.bfloat16
        )
        down_term = lax.dot_general(
            crossed_in, hidden_grad, (((0,), (0,)), ((), ())), preferred_element_type=jnp.float32
        )
        through = lax.dot_general(
            hidden_grad, down_full, (((1,), (1,)), ((), ())), preferred_element_type=jnp.float32
        )
        back = (back_wide + through).astype(jnp.bfloat16)
        up_parts[layer_index] = up_term
        down_parts[layer_index] = down_term
    row_total = lax.axis_size("row")
    width = first.shape[1]
    rank = up_parts[0].shape[1]
    block_rows = width // row_total
    piece = block_rows // groups
    slabs = jnp.stack(up_parts + down_parts).astype(jnp.bfloat16)
    count = slabs.shape[0]
    slabs = slabs.reshape(count, row_total, groups, piece, rank).transpose(0, 2, 1, 3, 4)
    group_part = lax.psum_scatter(
        slabs.reshape(count, width, rank), "group", scatter_dimension=1, tiled=True
    )
    first_grad = (first_grad + back.astype(jnp.float32)).astype(jnp.bfloat16)
    owner_grad = lax.all_to_all(first_grad, "group", split_axis=1, concat_axis=0, tiled=True)
    proj_term = lax.dot_general(
        ordered, owner_grad, (((0,), (0,)), ((), ())), preferred_element_type=jnp.float32
    )
    row_count_axis = lax.axis_size("row")
    bias_all = jnp.stack(bias_terms)
    proj_pieces = proj_term.reshape(row_count_axis, -1)
    bias_pieces = bias_all.reshape(layers, row_count_axis, -1).transpose(1, 0, 2)
    bias_pieces = bias_pieces.reshape(row_count_axis, -1)
    split = proj_pieces.shape[1]
    row_mine = jnp.sum(
        lax.all_to_all(jnp.concatenate([proj_pieces, bias_pieces], axis=1), "row", 0, 0, tiled=True),
        axis=0,
    )
    bias_chunk = exchange_sum(row_mine[split:], "group", groups)
    last = jnp.concatenate([row_mine[:split], bias_chunk])
    last_all = lax.all_to_all(
        jnp.broadcast_to(last[None], (row_count_axis,) + last.shape), "row", 0, 0, tiled=True
    )
    grad_proj = last_all[:, :split].reshape(proj_term.shape)
    grad_bias = (
        last_all[:, split:]
        .reshape(row_count_axis, layers, -1)
        .transpose(1, 0, 2)
        .reshape(bias_all.shape)
    )
    group_part, grad_proj, grad_bias = lax.optimization_barrier((group_part, grad_proj, grad_bias))
    row_pieces = group_part.reshape(count, row_total, piece, rank).transpose(1, 0, 2, 3)
    mine = jnp.sum(lax.all_to_all(row_pieces, "row", 0, 0, tiled=True).astype(jnp.float32), axis=0)
    spread = jnp.broadcast_to(mine[None], (groups,) + mine.shape)
    gathered = lax.all_to_all(spread, "group", 0, 0, tiled=True)
    blocks = gathered.transpose(1, 0, 2, 3).reshape(count, block_rows, rank)
    grad_up, grad_down = blocks[:layers], blocks[layers:]
    return (logits, grad_down, grad_up, grad_bias, grad_proj)


def solution(mesh):
    in_specs = (
        P("row", "group"),
        P("group"),
        P(),
        P(),
        P("group", None),
        P("row", None),
        P(None, "row", None),
        P(None, "row", None),
        P(),
        P(),
        P(("group", "row")),
    )
    out_specs = (
        P(("group", "row")),
        P(None, "row", None),
        P(None, "row", None),
        P(),
        P("group", None),
    )
    return jax.shard_map(body, mesh=mesh, in_specs=in_specs, out_specs=out_specs, check_vma=False)
```

```python
import jax
import jax.numpy as jnp
from jax import lax
from jax.sharding import PartitionSpec as P


def column_table(feature_id, lookup_table):
    columns = jnp.arange(lookup_table.shape[0], dtype=jnp.int32)
    picker = (feature_id[:, None] == columns[None, :]).astype(jnp.float32)
    return jnp.dot(picker, lookup_table, precision=lax.Precision.HIGHEST)


def exchange_sum(partial, axis, count):
    pieces = partial.reshape(count, -1)
    mine = jnp.sum(lax.all_to_all(pieces, axis, 0, 0, tiled=True), axis=0)
    spread = jnp.broadcast_to(mine[None], pieces.shape)
    return lax.all_to_all(spread, axis, 0, 0, tiled=True).reshape(partial.shape)


def group_all_reduce(rows, groups):
    stacked, height, width = rows.shape
    pieces = rows.reshape(stacked, groups, height // groups, width).transpose(1, 0, 2, 3)
    mine = jnp.sum(lax.all_to_all(pieces, "group", 0, 0, tiled=True).astype(jnp.float32), axis=0)
    spread = jnp.broadcast_to(mine[None], pieces.shape)
    gathered = lax.all_to_all(spread, "group", 0, 0, tiled=True)
    return gathered.transpose(1, 0, 2, 3).reshape(rows.shape)


def body(
    features,
    feature_id,
    feature_shift,
    feature_scale,
    proj_weight,
    row_slot,
    down_weight,
    up_weight,
    cross_bias,
    head_weight,
    labels,
):
    layers = down_weight.shape[0]
    groups = lax.axis_size("group")
    row_count = labels.shape[0]
    feature_stats = column_table(feature_id, jnp.stack([feature_shift, feature_scale], axis=1))
    normed = ((features - feature_stats[:, 0][None, :]) * feature_stats[:, 1][None, :]).astype(
        jnp.bfloat16
    )
    ordered = jnp.zeros_like(normed).at[row_slot[0]].set(normed)
    projected = jnp.dot(ordered, proj_weight, preferred_element_type=jnp.float32).astype(
        jnp.bfloat16
    )
    first = lax.all_to_all(projected, "group", split_axis=0, concat_axis=1, tiled=True)
    first_wide = first.astype(jnp.float32)
    crossed = first
    stored = []
    weights_full = lax.all_gather(
        jnp.concatenate([down_weight, up_weight], axis=0), "row", axis=1, tiled=True
    )
    for layer_index in range(layers):
        down_full, up_full = weights_full[layer_index], weights_full[layers + layer_index]
        hidden = jnp.dot(crossed, down_full, preferred_element_type=jnp.float32).astype(
            jnp.bfloat16
        )
        mixture = lax.dot_general(
            hidden, up_full, (((1,), (1,)), ((), ())), preferred_element_type=jnp.float32
        )
        mixture = mixture + cross_bias[layer_index][None, :]
        stored.append((crossed, hidden, mixture, down_full, up_full))
        crossed = (first_wide * mixture + crossed.astype(jnp.float32)).astype(jnp.bfloat16)
    logits = jnp.sum(crossed.astype(jnp.float32) * head_weight[None, :], axis=1)
    total_rows = row_count * groups * lax.axis_size("row")
    loss_scale = 2.0 * (crossed.shape[1] / total_rows) ** 0.5
    logit_grad = (jax.nn.sigmoid(logits) - labels.astype(jnp.float32)) * loss_scale
    back = (logit_grad[:, None] * head_weight[None, :]).astype(jnp.bfloat16)
    first_grad = jnp.zeros(first.shape, jnp.float32)
    up_parts = [None] * layers
    down_parts = [None] * layers
    bias_terms = [None] * layers
    for layer_index in reversed(range(layers)):
        crossed_in, hidden, mixture, down_full, up_full = stored[layer_index]
        back_wide = back.astype(jnp.float32)
        first_grad = first_grad + back_wide * mixture
        mix_grad = (back_wide * first_wide).astype(jnp.bfloat16)
        up_term = lax.dot_general(
            mix_grad, hidden, (((0,), (0,)), ((), ())), preferred_element_type=jnp.float32
        )
        bias_terms[layer_index] = mix_grad
        hidden_grad = jnp.dot(mix_grad, up_full, preferred_element_type=jnp.float32).astype(
            jnp.bfloat16
        )
        down_term = lax.dot_general(
            crossed_in, hidden_grad, (((0,), (0,)), ((), ())), preferred_element_type=jnp.float32
        )
        through = lax.dot_general(
            hidden_grad, down_full, (((1,), (1,)), ((), ())), preferred_element_type=jnp.float32
        )
        back = (back_wide + through).astype(jnp.bfloat16)
        up_parts[layer_index] = up_term
        down_parts[layer_index] = down_term
    slab = jnp.stack(up_parts + down_parts).astype(jnp.bfloat16)
    slab, bias_terms = lax.optimization_barrier((slab, bias_terms))
    bias_terms = [jnp.sum(mix_grad.astype(jnp.float32), axis=0) for mix_grad in bias_terms]
    weight_rows = lax.psum_scatter(slab, "row", scatter_dimension=1, tiled=True)
    first_grad = (first_grad + back.astype(jnp.float32)).astype(jnp.bfloat16)
    owner_grad = lax.all_to_all(first_grad, "group", split_axis=1, concat_axis=0, tiled=True)
    proj_term = lax.dot_general(
        ordered, owner_grad, (((0,), (0,)), ((), ())), preferred_element_type=jnp.float32
    )
    row_count_axis = lax.axis_size("row")
    bias_all = jnp.stack(bias_terms)
    proj_pieces = proj_term.reshape(row_count_axis, -1)
    bias_pieces = bias_all.reshape(layers, row_count_axis, -1).transpose(1, 0, 2)
    bias_pieces = bias_pieces.reshape(row_count_axis, -1)
    split = proj_pieces.shape[1]
    row_mine = jnp.sum(
        lax.all_to_all(jnp.concatenate([proj_pieces, bias_pieces], axis=1), "row", 0, 0, tiled=True),
        axis=0,
    )
    bias_chunk = exchange_sum(row_mine[split:], "group", groups)
    last = jnp.concatenate([row_mine[:split], bias_chunk])
    last_all = lax.all_to_all(
        jnp.broadcast_to(last[None], (row_count_axis,) + last.shape), "row", 0, 0, tiled=True
    )
    grad_proj = last_all[:, :split].reshape(proj_term.shape)
    grad_bias = (
        last_all[:, split:]
        .reshape(row_count_axis, layers, -1)
        .transpose(1, 0, 2)
        .reshape(bias_all.shape)
    )
    weight_rows, grad_proj, grad_bias = lax.optimization_barrier((weight_rows, grad_proj, grad_bias))
    weight_sums = group_all_reduce(weight_rows, groups)
    grad_up, grad_down = weight_sums[:layers], weight_sums[layers:]
    return (logits, grad_down, grad_up, grad_bias, grad_proj)


def solution(mesh):
    in_specs = (
        P("row", "group"),
        P("group"),
        P(),
        P(),
        P("group", None),
        P("row", None),
        P(None, "row", None),
        P(None, "row", None),
        P(),
        P(),
        P(("group", "row")),
    )
    out_specs = (
        P(("group", "row")),
        P(None, "row", None),
        P(None, "row", None),
        P(),
        P("group", None),
    )
    return jax.shard_map(body, mesh=mesh, in_specs=in_specs, out_specs=out_specs, check_vma=False)
```

```python
import jax
import jax.numpy as jnp
from jax import lax
from jax.sharding import PartitionSpec as P


def column_table(feature_id, lookup_table):
    columns = jnp.arange(lookup_table.shape[0], dtype=jnp.int32)
    picker = (feature_id[:, None] == columns[None, :]).astype(jnp.float32)
    return jnp.dot(picker, lookup_table, precision=lax.Precision.HIGHEST)


def exchange_sum(partial, axis, count):
    pieces = partial.reshape(count, -1)
    mine = jnp.sum(lax.all_to_all(pieces, axis, 0, 0, tiled=True), axis=0)
    spread = jnp.broadcast_to(mine[None], pieces.shape)
    return lax.all_to_all(spread, axis, 0, 0, tiled=True).reshape(partial.shape)


def group_all_reduce(rows, groups):
    stacked, height, width = rows.shape
    pieces = rows.reshape(stacked, groups, height // groups, width).transpose(1, 0, 2, 3)
    mine = jnp.sum(lax.all_to_all(pieces, "group", 0, 0, tiled=True).astype(jnp.float32), axis=0)
    spread = jnp.broadcast_to(mine.astype(jnp.bfloat16)[None], pieces.shape)
    gathered = lax.all_to_all(spread, "group", 0, 0, tiled=True).astype(jnp.float32)
    return gathered.transpose(1, 0, 2, 3).reshape(rows.shape)


def body(
    features,
    feature_id,
    feature_shift,
    feature_scale,
    proj_weight,
    row_slot,
    down_weight,
    up_weight,
    cross_bias,
    head_weight,
    labels,
):
    layers = down_weight.shape[0]
    groups = lax.axis_size("group")
    row_count = labels.shape[0]
    feature_stats = column_table(feature_id, jnp.stack([feature_shift, feature_scale], axis=1))
    normed = ((features - feature_stats[:, 0][None, :]) * feature_stats[:, 1][None, :]).astype(
        jnp.bfloat16
    )
    ordered = jnp.zeros_like(normed).at[row_slot[0]].set(normed)
    projected = jnp.dot(ordered, proj_weight, preferred_element_type=jnp.float32).astype(
        jnp.bfloat16
    )
    first = lax.all_to_all(projected, "group", split_axis=0, concat_axis=1, tiled=True)
    first_wide = first.astype(jnp.float32)
    crossed = first
    stored = []
    weights_full = lax.all_gather(
        jnp.concatenate([down_weight, up_weight], axis=0), "row", axis=1, tiled=True
    )
    for layer_index in range(layers):
        down_full, up_full = weights_full[layer_index], weights_full[layers + layer_index]
        hidden = jnp.dot(crossed, down_full, preferred_element_type=jnp.float32).astype(
            jnp.bfloat16
        )
        mixture = lax.dot_general(
            hidden, up_full, (((1,), (1,)), ((), ())), preferred_element_type=jnp.float32
        )
        mixture = mixture + cross_bias[layer_index][None, :]
        stored.append((crossed, hidden, mixture, down_full, up_full))
        crossed = (first_wide * mixture + crossed.astype(jnp.float32)).astype(jnp.bfloat16)
    logits = jnp.sum(crossed.astype(jnp.float32) * head_weight[None, :], axis=1)
    total_rows = row_count * groups * lax.axis_size("row")
    loss_scale = 2.0 * (crossed.shape[1] / total_rows) ** 0.5
    logit_grad = (jax.nn.sigmoid(logits) - labels.astype(jnp.float32)) * loss_scale
    back = (logit_grad[:, None] * head_weight[None, :]).astype(jnp.bfloat16)
    first_grad = jnp.zeros(first.shape, jnp.float32)
    up_parts = [None] * layers
    down_parts = [None] * layers
    bias_terms = [None] * layers
    for layer_index in reversed(range(layers)):
        crossed_in, hidden, mixture, down_full, up_full = stored[layer_index]
        back_wide = back.astype(jnp.float32)
        first_grad = first_grad + back_wide * mixture
        mix_grad = (back_wide * first_wide).astype(jnp.bfloat16)
        up_term = lax.dot_general(
            mix_grad, hidden, (((0,), (0,)), ((), ())), preferred_element_type=jnp.float32
        )
        bias_terms[layer_index] = mix_grad
        hidden_grad = jnp.dot(mix_grad, up_full, preferred_element_type=jnp.float32).astype(
            jnp.bfloat16
        )
        down_term = lax.dot_general(
            crossed_in, hidden_grad, (((0,), (0,)), ((), ())), preferred_element_type=jnp.float32
        )
        through = lax.dot_general(
            hidden_grad, down_full, (((1,), (1,)), ((), ())), preferred_element_type=jnp.float32
        )
        back = (back_wide + through).astype(jnp.bfloat16)
        up_parts[layer_index] = up_term
        down_parts[layer_index] = down_term
    slab = jnp.stack(up_parts + down_parts).astype(jnp.bfloat16)
    slab, bias_terms = lax.optimization_barrier((slab, bias_terms))
    bias_terms = [jnp.sum(mix_grad.astype(jnp.float32), axis=0) for mix_grad in bias_terms]
    weight_rows = lax.psum_scatter(slab, "row", scatter_dimension=1, tiled=True)
    first_grad = (first_grad + back.astype(jnp.float32)).astype(jnp.bfloat16)
    owner_grad = lax.all_to_all(first_grad, "group", split_axis=1, concat_axis=0, tiled=True)
    proj_term = lax.dot_general(
        ordered, owner_grad, (((0,), (0,)), ((), ())), preferred_element_type=jnp.float32
    )
    row_count_axis = lax.axis_size("row")
    bias_all = jnp.stack(bias_terms)
    proj_pieces = proj_term.reshape(row_count_axis, -1)
    bias_pieces = bias_all.reshape(layers, row_count_axis, -1).transpose(1, 0, 2)
    bias_pieces = bias_pieces.reshape(row_count_axis, -1)
    split = proj_pieces.shape[1]
    row_mine = jnp.sum(
        lax.all_to_all(jnp.concatenate([proj_pieces, bias_pieces], axis=1), "row", 0, 0, tiled=True),
        axis=0,
    )
    bias_chunk = exchange_sum(row_mine[split:], "group", groups)
    last = jnp.concatenate([row_mine[:split], bias_chunk])
    last_all = lax.all_to_all(
        jnp.broadcast_to(last[None], (row_count_axis,) + last.shape), "row", 0, 0, tiled=True
    )
    grad_proj = last_all[:, :split].reshape(proj_term.shape)
    grad_bias = (
        last_all[:, split:]
        .reshape(row_count_axis, layers, -1)
        .transpose(1, 0, 2)
        .reshape(bias_all.shape)
    )
    weight_rows, grad_proj, grad_bias = lax.optimization_barrier((weight_rows, grad_proj, grad_bias))
    weight_sums = group_all_reduce(weight_rows, groups)
    grad_up, grad_down = weight_sums[:layers], weight_sums[layers:]
    return (logits, grad_down, grad_up, grad_bias, grad_proj)


def solution(mesh):
    in_specs = (
        P("row", "group"),
        P("group"),
        P(),
        P(),
        P("group", None),
        P("row", None),
        P(None, "row", None),
        P(None, "row", None),
        P(),
        P(),
        P(("group", "row")),
    )
    out_specs = (
        P(("group", "row")),
        P(None, "row", None),
        P(None, "row", None),
        P(),
        P("group", None),
    )
    return jax.shard_map(body, mesh=mesh, in_specs=in_specs, out_specs=out_specs, check_vma=False)
```
